256 devices in a mesh: blk: 16 (over z, x_lo), inner: 16 (over y, x_hi, core).
Axes of the slice: x: 4 (x_hi: 2, x_lo: 2; x = x_hi * 2 + x_lo), y: 4, z: 8, core: 2. Of those that a mesh axis runs over, the one named last changes fastest.
Arguments:
- tokens: bfloat16 [32768, 4096], P(('blk', 'inner')), may hold values from -6 to 6
- expert_ids: int32 [32768, 8], P(('blk', 'inner')), may hold values from 0 to 127, all different within a row; in each aligned block of 128 rows (0 to 127, 128 to 255, ...) at most 12 rows name the same one
- route_weights: float32 [32768, 8], P(('blk', 'inner')), may hold values from 0.1 to 1
- w_in: bfloat16 [256, 4096, 768], P(('blk', 'inner')), may hold values from -0.09375 to 0.09375
- w_out: bfloat16 [256, 384, 4096], P(('blk', 'inner')), may hold values from -0.3125 to 0.3125
Outputs:
- moe_out: bfloat16 [32768, 4096], P(('blk', 'inner'))
The draws below stay inside these ranges and needn't reach their ends.
Inputs may be any that keep to these rules, and one draw needn't show every extreme that they name: `expert_ids`: each row names 8 different experts; among the 128 rows of one device no expert is named more than 12 times, a bound that some block reaches.
All inputs are finite; a program needn't handle non-finite values.
Results may differ from the reference program's by a relative error of at most 0.0085.
Values may be sent and summed in bfloat16 or wider, within the bound.
No kernel may reach another device: no remote copies, remote signals or barrier semaphores. Data moves between devices by JAX's collectives and lax.ppermute only.
A program may use at most 128 MiB of HBM per device.

```python
import math
import jax
import jax.numpy as jnp
import numpy as np
from jax import lax

D = 4096
TOPK = 8
SPLIT = 2
STEPS = 3
TOK_DEV = 128
H_DEV = 384
EXP_GRP = 8
EXPERTS = 128
CAP = 12
TOKENS = 32768
N_BLK = 16
N_INNER = 16


def block_levels(stream_key, extent, cuts, low, high):
    loudness, own = 1.0, jax.random.fold_in(stream_key, 6)
    for position, parts in cuts:
        steps = jnp.exp(jax.random.uniform(jax.random.fold_in(own, position), (parts,), jnp.float32, low / len(cuts), high / len(cuts)))
        loudness = loudness * jnp.repeat(steps, extent[position] // parts).reshape([-1 if axis == position else 1 for axis in range(len(extent))])
    return loudness


def assign_block(rng, own, number, rows, number_of, top, limit, lean):
    order = jax.random.permutation(rng, number_of)
    heavy_load, common = portions_of(number_of, rows * top, limit, lean, True), portions_of(number_of, rows * top, limit, lean, False)
    places = jnp.arange(number_of)

    def named(lengths, turn):
        used = int((lengths > 0).sum())
        fixed = max(1, used // 4)
        shifted = fixed + (places - fixed + turn * (used - fixed)) % max(1, number_of - fixed)
        return jnp.zeros((number_of,), jnp.int32).at[order[jnp.where(places < fixed, places, shifted)]].set(jnp.asarray(lengths, jnp.int32))

    lengths = jnp.where(number % 4 == 0, named(heavy_load, number // 4), named(common, number - number // 4 - 1))
    mixed = jax.random.permutation(jax.random.fold_in(own, 3), number_of)
    source_of, receiver = mixed[0:number_of // 2 * 2:2], mixed[1:number_of // 2 * 2:2]
    slack = jnp.minimum(lengths[source_of] - 1, limit - lengths[receiver]) // 2
    slack = jnp.where((source_of == order[0]) | (receiver == order[0]) | (lengths[receiver] == 0), 0, jnp.maximum(slack, 0))
    shifted = jax.random.randint(jax.random.fold_in(own, 4), (number_of // 2,), 0, 1 << 20) % (slack + 1)
    lengths = lengths.at[source_of].add(-shifted).at[receiver].add(shifted)
    members = jnp.searchsorted(jnp.cumsum(lengths), jnp.arange(rows * top), side="right").astype(jnp.int32)
    grid = members.reshape(top, rows).T
    grid = grid[jax.random.permutation(jax.random.fold_in(own, 1), rows)]
    turn = jax.random.randint(jax.random.fold_in(own, 2), (rows, 1), 0, top)
    return jnp.take_along_axis(grid, (jnp.arange(top)[None, :] + turn) % top, axis=1)


def portions_of(count, total, limit, lean, full):
    loads = [(1 << 20) // math.isqrt(rank ** lean) + 1 for rank in range(1, count + 1)]
    largest = limit if full else min(limit, max(-(-total // count), total * loads[0] // sum(loads)))
    least = 1 if total - largest >= count - 1 else 0
    holding, surplus = [largest] + [least] * (count - 1), total - largest - least * (count - 1)
    while surplus > 0:
        free = [i for i in range(1, count) if holding[i] < largest] or [i for i in range(1, count) if holding[i] < limit]
        whole, remaining = sum([loads[i] for i in free]), surplus
        for i in free:
            extra = min(limit - holding[i], max(1, remaining * loads[i] // whole), surplus)
            holding[i] = holding[i] + extra
            surplus = surplus - extra
    return np.array(holding)


def scatter_about(stream_key, shape, scale, limit, pieces=(), held_as=jnp.bfloat16):
    array = scale * jax.random.normal(stream_key, shape, jnp.float32)
    if pieces:
        array = array * block_levels(stream_key, shape, pieces, -0.22, 0.18)
    return jnp.clip(array, -limit, limit).astype(held_as)


def setup_inputs(seed: int = 0) -> dict:
    seeds = jax.random.split(jax.random.key(seed), 6)
    tokens = scatter_about(seeds[0], (TOKENS, D), 1.0, 6.0, ((0, 256),))
    expert_ids_keys = jax.random.split(jax.random.fold_in(seeds[1], 1), TOKENS // TOK_DEV)
    expert_ids_turns = jax.random.permutation(jax.random.fold_in(seeds[1], 3), TOKENS // TOK_DEV)
    expert_ids = jax.vmap(lambda own, number: assign_block(jax.random.fold_in(seeds[1], 2), own, number, TOK_DEV, EXPERTS, TOPK, CAP, 2))(expert_ids_keys, expert_ids_turns).reshape((TOKENS, TOPK))
    route_weights = jnp.clip(jnp.exp(math.log(1.0) - 2.3025851 * jax.random.uniform(seeds[2], (TOKENS, TOPK), jnp.float32) ** block_levels(seeds[2], (TOKENS, TOPK), ((0, 256),), -0.2, 0.2)), 0.1, 1.0)
    w_in = scatter_about(seeds[3], (EXPERTS * SPLIT, D, 2 * H_DEV), D ** -0.5, 0.09375, ((0, 256),))
    w_out = scatter_about(seeds[4], (EXPERTS * SPLIT, H_DEV, D), H_DEV ** -0.5, 0.3125, ((0, 256),))
    return {"tokens": tokens, "expert_ids": expert_ids, "route_weights": route_weights, "w_in": w_in, "w_out": w_out}


def reference(tokens, expert_ids, route_weights, w_in, w_out):
    group_of = jnp.arange(TOKENS, dtype=jnp.int32) // (N_INNER * TOK_DEV)
    home_group = expert_ids // EXP_GRP
    counted = jnp.mod(group_of[:, None] - home_group, N_BLK) < STEPS
    max_rows = STEPS * N_INNER * CAP

    def one_expert(accumulated, expert):
        member = counted & (expert_ids == expert)
        weight = jnp.sum(jnp.where(member, route_weights, jnp.zeros_like(route_weights)), axis=1)
        chosen = jnp.any(member, axis=1)
        row_count = jnp.sum(chosen.astype(jnp.int32))
        row_index = jnp.nonzero(chosen, size=max_rows, fill_value=0)[0].astype(jnp.int32)
        live_rows = jnp.arange(max_rows, dtype=jnp.int32) < row_count
        row_scale = jnp.where(live_rows, weight[row_index], jnp.zeros_like(weight[row_index]))
        gathered = tokens[row_index]
        mixture = jnp.zeros((max_rows, D), jnp.float32)
        for half_index in range(SPLIT):
            slice_index = expert * SPLIT + half_index
            projected = jnp.dot(gathered, w_in[slice_index], preferred_element_type=jnp.float32)
            activated = (jax.nn.silu(projected[:, :H_DEV]) * projected[:, H_DEV:]).astype(jnp.bfloat16)
            partial_value = jnp.dot(activated, w_out[slice_index], preferred_element_type=jnp.float32).astype(jnp.bfloat16)
            partial_value = lax.optimization_barrier(partial_value)
            mixture = mixture + partial_value.astype(jnp.float32)
        accumulated = accumulated.at[row_index].add(row_scale[:, None] * mixture)
        return accumulated, None

    accumulated, _ = lax.scan(one_expert, jnp.zeros((TOKENS, D), jnp.float32), jnp.arange(EXPERTS, dtype=jnp.int32))
    return accumulated.astype(jnp.bfloat16)
```

```python
import jax
import jax.numpy as jnp
from jax import lax
from jax.sharding import PartitionSpec as P

TOPK = 8
SPLIT = 2
STEPS = 3


def shifted(value, axis, steps):
    count = lax.axis_size(axis)
    pairs = [(source, (source + steps) % count) for source in range(count)]
    return lax.ppermute(value, axis, pairs)


def swapped_with_partner(value, axis):
    count = lax.axis_size(axis)
    pairs = [(source, source ^ 1) for source in range(count)]
    return lax.ppermute(value, axis, pairs)


def whole_expert(rows, w_in_a, w_out_a, w_in_b, w_out_b):
    hidden = w_out_a.shape[0]

    def one_half(w_in_now, w_out_now):
        projected = jnp.dot(rows, w_in_now, preferred_element_type=jnp.float32)
        activated = (jax.nn.silu(projected[:, :hidden]) * projected[:, hidden:]).astype(
            jnp.bfloat16
        )
        return jnp.dot(activated, w_out_now, preferred_element_type=jnp.float32)

    return (one_half(w_in_a, w_out_a) + one_half(w_in_b, w_out_b)).astype(jnp.bfloat16)


def on_device(tokens, expert_ids, route_weights, w_in, w_out):
    inner_count = lax.axis_size("inner")
    blk_count = lax.axis_size("blk")
    group_index = lax.axis_index("blk")
    group_count = inner_count // SPLIT
    tok_rows, width = tokens.shape
    experts_all = group_count * blk_count
    capacity = max(2, 3 * tok_rows * TOPK // (2 * experts_all))
    capacity = -(-capacity // SPLIT) * SPLIT
    half_cap = capacity // SPLIT

    w_in_other = swapped_with_partner(w_in, "inner")
    w_out_other = swapped_with_partner(w_out, "inner")

    homes = jnp.mod(group_index - jnp.arange(STEPS, dtype=jnp.int32), blk_count)
    targets = (
        homes[:, None] * group_count + jnp.arange(group_count, dtype=jnp.int32)[None, :]
    ).reshape(-1)
    matches = expert_ids[:, :, None] == targets[None, None, :]
    chosen = jnp.any(matches, axis=1).astype(jnp.int32)
    weighting = jnp.sum(jnp.where(matches, route_weights[:, :, None], 0.0), axis=1)
    position = jnp.cumsum(chosen, axis=0) - chosen
    slot_ids = jnp.arange(capacity, dtype=jnp.int32)
    one_hot = (chosen.T[:, None, :] == 1) & (position.T[:, None, :] == slot_ids[None, :, None])
    one_hot = one_hot.reshape(STEPS, group_count, SPLIT, half_cap, tok_rows).transpose(
        1, 2, 0, 3, 4
    )
    scale = jnp.where(
        one_hot,
        weighting.T.reshape(STEPS, group_count, 1, 1, tok_rows).transpose(1, 2, 0, 3, 4),
        0.0,
    )
    picked = jnp.einsum(
        "qcrht,td->qcrhd",
        one_hot.astype(jnp.bfloat16),
        tokens,
        preferred_element_type=jnp.float32,
    ).astype(jnp.bfloat16)
    outgoing = picked.reshape(inner_count, STEPS, half_cap, width)

    arrived = lax.all_to_all(outgoing, "inner", split_axis=0, concat_axis=0, tiled=True)
    parts = [arrived[:, 0]]
    for rotation in range(1, STEPS):
        parts.append(shifted(arrived[:, rotation], "blk", -rotation))

    results = []
    for rotation in range(STEPS):
        rows = parts[rotation].reshape(inner_count * half_cap, width)
        done = whole_expert(rows, w_in[0], w_out[0], w_in_other[0], w_out_other[0])
        done = done.reshape(inner_count, half_cap, width)
        if rotation > 0:
            done = shifted(done, "blk", rotation)
        results.append(done)
    returned = jnp.stack(results, axis=1)
    returned = lax.all_to_all(returned, "inner", split_axis=0, concat_axis=0, tiled=True)
    returned = returned.reshape(group_count, SPLIT, STEPS, half_cap, width)

    scale_hi = scale.astype(jnp.bfloat16)
    scale_lo = (scale - scale_hi.astype(jnp.float32)).astype(jnp.bfloat16)
    combined = jnp.einsum(
        "qcrht,qcrhd->td", scale_hi, returned, preferred_element_type=jnp.float32
    ) + jnp.einsum("qcrht,qcrhd->td", scale_lo, returned, preferred_element_type=jnp.float32)
    return combined.astype(jnp.bfloat16)


def solution(mesh):
    return jax.shard_map(
        on_device,
        mesh=mesh,
        in_specs=(
            P(("blk", "inner"), None),
            P(("blk", "inner"), None),
            P(("blk", "inner"), None),
            P(("blk", "inner"), None, None),
            P(("blk", "inner"), None, None),
        ),
        out_specs=P(("blk", "inner"), None),
        check_vma=False,
    )
```

```python
import jax
import jax.numpy as jnp
from jax import lax
from jax.sharding import PartitionSpec as P

TOPK = 8
SPLIT = 2
STEPS = 3


def shifted(value, axis, steps):
    count = lax.axis_size(axis)
    pairs = [(source, (source + steps) % count) for source in range(count)]
    return lax.ppermute(value, axis, pairs)


def swapped_with_partner(value, axis):
    count = lax.axis_size(axis)
    pairs = [(source, source ^ 1) for source in range(count)]
    return lax.ppermute(value, axis, pairs)


def whole_expert(rows, w_in_a, w_out_a, w_in_b, w_out_b):
    hidden = w_out_a.shape[0]

    def one_half(w_in_now, w_out_now):
        projected = jnp.dot(rows, w_in_now, preferred_element_type=jnp.float32)
        activated = (jax.nn.silu(projected[:, :hidden]) * projected[:, hidden:]).astype(
            jnp.bfloat16
        )
        return jnp.dot(activated, w_out_now, preferred_element_type=jnp.float32)

    return (one_half(w_in_a, w_out_a) + one_half(w_in_b, w_out_b)).astype(jnp.bfloat16)


def on_device(tokens, expert_ids, route_weights, w_in, w_out):
    inner_count = lax.axis_size("inner")
    blk_count = lax.axis_size("blk")
    group_index = lax.axis_index("blk")
    group_count = inner_count // SPLIT
    tok_rows, width = tokens.shape
    experts_all = group_count * blk_count
    capacity = max(2, 3 * tok_rows * TOPK // (2 * experts_all))
    capacity = -(-capacity // SPLIT) * SPLIT
    half_cap = capacity // SPLIT

    w_in_other = swapped_with_partner(w_in, "inner")
    w_out_other = swapped_with_partner(w_out, "inner")

    homes = jnp.mod(group_index - jnp.arange(STEPS, dtype=jnp.int32), blk_count)
    targets = (
        homes[:, None] * group_count + jnp.arange(group_count, dtype=jnp.int32)[None, :]
    ).reshape(-1)
    matches = expert_ids[:, :, None] == targets[None, None, :]
    chosen = jnp.any(matches, axis=1).astype(jnp.int32)
    weighting = jnp.sum(jnp.where(matches, route_weights[:, :, None], 0.0), axis=1)
    position = jnp.cumsum(chosen, axis=0) - chosen
    slot_ids = jnp.arange(capacity, dtype=jnp.int32)
    one_hot = (chosen.T[:, None, :] == 1) & (position.T[:, None, :] == slot_ids[None, :, None])
    one_hot = one_hot.reshape(STEPS, group_count, SPLIT, half_cap, tok_rows)
    scale = jnp.where(
        one_hot, weighting.T.reshape(STEPS, group_count, 1, 1, tok_rows), 0.0
    )
    scale_hi = scale.astype(jnp.bfloat16)
    scale_lo = (scale - scale_hi.astype(jnp.float32)).astype(jnp.bfloat16)
    picked = jnp.einsum(
        "rqcht,td->rqchd",
        one_hot.astype(jnp.bfloat16),
        tokens,
        preferred_element_type=jnp.float32,
    ).astype(jnp.bfloat16)

    arrived = [None] * STEPS
    for rotation in reversed(range(STEPS)):
        outgoing = picked[rotation].reshape(inner_count, half_cap, width)
        here = lax.all_to_all(outgoing, "inner", split_axis=0, concat_axis=0, tiled=True)
        if rotation > 0:
            here = shifted(here, "blk", -rotation)
        arrived[rotation] = here

    combined = jnp.zeros((tok_rows, width), jnp.float32)
    for rotation in range(STEPS):
        rows = arrived[rotation].reshape(inner_count * half_cap, width)
        done = whole_expert(rows, w_in[0], w_out[0], w_in_other[0], w_out_other[0])
        done = done.reshape(inner_count, half_cap, width)
        if rotation > 0:
            done = shifted(done, "blk", rotation)
        back = lax.all_to_all(done, "inner", split_axis=0, concat_axis=0, tiled=True)
        back = back.reshape(group_count, SPLIT, half_cap, width)
        combined = combined + jnp.einsum(
            "qcht,qchd->td", scale_hi[rotation], back, preferred_element_type=jnp.float32
        )
        combined = combined + jnp.einsum(
            "qcht,qchd->td", scale_lo[rotation], back, preferred_element_type=jnp.float32
        )
    return combined.astype(jnp.bfloat16)


def solution(mesh):
    return jax.shard_map(
        on_device,
        mesh=mesh,
        in_specs=(
            P(("blk", "inner"), None),
            P(("blk", "inner"), None),
            P(("blk", "inner"), None),
            P(("blk", "inner"), None, None),
            P(("blk", "inner"), None, None),
        ),
        out_specs=P(("blk", "inner"), None),
        check_vma=False,
    )
```

```python
import jax
import jax.numpy as jnp
from jax import lax
from jax.sharding import PartitionSpec as P

TOPK = 8
SPLIT = 2
STEPS = 3


def shifted(value, axis, steps):
    count = lax.axis_size(axis)
    pairs = [(source, (source + steps) % count) for source in range(count)]
    return lax.ppermute(value, axis, pairs)


def swapped_with_partner(value, axis):
    count = lax.axis_size(axis)
    pairs = [(source, source ^ 1) for source in range(count)]
    return lax.ppermute(value, axis, pairs)


def whole_expert(rows, w_in_a, w_out_a, w_in_b, w_out_b):
    hidden = w_out_a.shape[0]

    def one_half(w_in_now, w_out_now):
        projected = jnp.dot(rows, w_in_now, preferred_element_type=jnp.float32)
        activated = (jax.nn.silu(projected[:, :hidden]) * projected[:, hidden:]).astype(
            jnp.bfloat16
        )
        return jnp.dot(activated, w_out_now, preferred_element_type=jnp.float32)

    return (one_half(w_in_a, w_out_a) + one_half(w_in_b, w_out_b)).astype(jnp.bfloat16)


def on_device(tokens, expert_ids, route_weights, w_in, w_out):
    inner_count = lax.axis_size("inner")
    blk_count = lax.axis_size("blk")
    group_index = lax.axis_index("blk")
    group_count = inner_count // SPLIT
    tok_rows, width = tokens.shape
    experts_all = group_count * blk_count
    capacity = max(2, 3 * tok_rows * TOPK // (2 * experts_all))
    capacity = -(-capacity // SPLIT) * SPLIT
    half_cap = capacity // SPLIT

    w_in_other = swapped_with_partner(w_in, "inner")
    w_out_other = swapped_with_partner(w_out, "inner")

    homes = jnp.mod(group_index - jnp.arange(STEPS, dtype=jnp.int32), blk_count)
    targets = (
        homes[:, None] * group_count + jnp.arange(group_count, dtype=jnp.int32)[None, :]
    ).reshape(-1)
    matches = expert_ids[:, :, None] == targets[None, None, :]
    chosen = jnp.any(matches, axis=1).astype(jnp.int32)
    weighting = jnp.sum(jnp.where(matches, route_weights[:, :, None], 0.0), axis=1)
    position = jnp.cumsum(chosen, axis=0) - chosen
    slot_ids = jnp.arange(capacity, dtype=jnp.int32)
    one_hot = (chosen.T[:, None, :] == 1) & (position.T[:, None, :] == slot_ids[None, :, None])
    one_hot = one_hot.reshape(STEPS, group_count, SPLIT, half_cap, tok_rows)
    scale = jnp.where(
        one_hot, weighting.T.reshape(STEPS, group_count, 1, 1, tok_rows), 0.0
    )
    scale_hi = scale.astype(jnp.bfloat16)
    scale_lo = (scale - scale_hi.astype(jnp.float32)).astype(jnp.bfloat16)
    lanes_major = width // 128
    dense = tokens.reshape(tok_rows, lanes_major, 128)
    picked = jnp.einsum(
        "rqcht,tkl->qcrhkl",
        one_hot.astype(jnp.bfloat16),
        dense,
        preferred_element_type=jnp.float32,
    ).astype(jnp.bfloat16)
    outgoing = picked.reshape(inner_count, STEPS * half_cap * lanes_major, 128)
    arrived = lax.all_to_all(outgoing, "inner", split_axis=0, concat_axis=0, tiled=True)
    arrived = arrived.reshape(inner_count, STEPS, half_cap, lanes_major, 128)

    parts = []
    for rotation in range(STEPS):
        part = arrived[:, rotation]
        if rotation > 0:
            part = shifted(part, "blk", -rotation)
        parts.append(part.reshape(inner_count * half_cap, width))
    rows = jnp.concatenate(parts, axis=0)
    done = whole_expert(rows, w_in[0], w_out[0], w_in_other[0], w_out_other[0])
    done = done.reshape(STEPS, inner_count, half_cap, lanes_major, 128)

    results = []
    for rotation in range(STEPS):
        result = done[rotation]
        if rotation > 0:
            result = shifted(result, "blk", rotation)
        results.append(result)
    returned = jnp.stack(results, axis=1)
    returned = returned.reshape(inner_count, STEPS * half_cap * lanes_major, 128)
    returned = lax.all_to_all(returned, "inner", split_axis=0, concat_axis=0, tiled=True)
    returned = returned.reshape(group_count, SPLIT, STEPS, half_cap, lanes_major, 128)

    combined = jnp.einsum(
        "rqcht,qcrhkl->tkl", scale_hi, returned, preferred_element_type=jnp.float32
    ) + jnp.einsum("rqcht,qcrhkl->tkl", scale_lo, returned, preferred_element_type=jnp.float32)
    combined = combined.reshape(tok_rows, width)
    return combined.astype(jnp.bfloat16)


def solution(mesh):
    return jax.shard_map(
        on_device,
        mesh=mesh,
        in_specs=(
            P(("blk", "inner"), None),
            P(("blk", "inner"), None),
            P(("blk", "inner"), None),
            P(("blk", "inner"), None, None),
            P(("blk", "inner"), None, None),
        ),
        out_specs=P(("blk", "inner"), None),
        check_vma=False,
    )
```

```python
import jax
import jax.numpy as jnp
from jax import lax
from jax.sharding import PartitionSpec as P

TOPK = 8
SPLIT = 2
STEPS = 3


def shifted(value, axis, steps):
    count = lax.axis_size(axis)
    pairs = [(source, (source + steps) % count) for source in range(count)]
    return lax.ppermute(value, axis, pairs)


def swapped_with_partner(value, axis):
    count = lax.axis_size(axis)
    pairs = [(source, source ^ 1) for source in range(count)]
    return lax.ppermute(value, axis, pairs)


def whole_expert(rows, w_in_a, w_out_a, w_in_b, w_out_b):
    hidden = w_out_a.shape[0]

    def one_half(w_in_now, w_out_now):
        projected = jnp.dot(rows, w_in_now, preferred_element_type=jnp.float32)
        activated = (jax.nn.silu(projected[:, :hidden]) * projected[:, hidden:]).astype(
            jnp.bfloat16
        )
        return jnp.dot(activated, w_out_now, preferred_element_type=jnp.float32)

    return (one_half(w_in_a, w_out_a) + one_half(w_in_b, w_out_b)).astype(jnp.bfloat16)


def on_device(tokens, expert_ids, route_weights, w_in, w_out):
    inner_count = lax.axis_size("inner")
    blk_count = lax.axis_size("blk")
    group_index = lax.axis_index("blk")
    group_count = inner_count // SPLIT
    tok_rows, width = tokens.shape
    experts_all = group_count * blk_count
    capacity = max(2, 3 * tok_rows * TOPK // (2 * experts_all))
    capacity = -(-capacity // SPLIT) * SPLIT
    half_cap = capacity // SPLIT

    w_in_other = swapped_with_partner(w_in, "inner")
    w_out_other = swapped_with_partner(w_out, "inner")

    homes = jnp.mod(group_index - jnp.arange(STEPS, dtype=jnp.int32), blk_count)
    targets = (
        homes[:, None] * group_count + jnp.arange(group_count, dtype=jnp.int32)[None, :]
    ).reshape(-1)
    matches = expert_ids[:, :, None] == targets[None, None, :]
    chosen = jnp.any(matches, axis=1).astype(jnp.int32)
    weighting = jnp.sum(jnp.where(matches, route_weights[:, :, None], 0.0), axis=1)
    position = jnp.cumsum(chosen, axis=0) - chosen
    slot_ids = jnp.arange(capacity, dtype=jnp.int32)
    one_hot = (chosen.T[:, None, :] == 1) & (position.T[:, None, :] == slot_ids[None, :, None])
    one_hot = one_hot.reshape(STEPS, group_count, SPLIT, half_cap, tok_rows)
    scale = jnp.where(
        one_hot, weighting.T.reshape(STEPS, group_count, 1, 1, tok_rows), 0.0
    )
    scale_hi = scale.astype(jnp.bfloat16)
    scale_lo = (scale - scale_hi.astype(jnp.float32)).astype(jnp.bfloat16)
    lanes_major = width // 128
    dense = tokens.reshape(tok_rows, lanes_major, 128)
    picked = jnp.einsum(
        "rqcht,tkl->rqchkl",
        one_hot.astype(jnp.bfloat16),
        dense,
        preferred_element_type=jnp.float32,
    ).astype(jnp.bfloat16)

    arrived = [None] * STEPS
    for rotation in reversed(range(STEPS)):
        outgoing = picked[rotation].reshape(inner_count, half_cap, lanes_major, 128)
        if rotation > 0:
            outgoing = shifted(outgoing, "blk", -rotation)
        arrived[rotation] = lax.all_to_all(
            outgoing, "inner", split_axis=0, concat_axis=0, tiled=True
        )
    rows = jnp.concatenate([part.reshape(-1, width) for part in arrived], axis=0)
    done = whole_expert(rows, w_in[0], w_out[0], w_in_other[0], w_out_other[0])
    done = done.reshape(STEPS, inner_count, half_cap, lanes_major, 128)

    combined = jnp.zeros((tok_rows, lanes_major, 128), jnp.float32)
    for rotation in reversed(range(STEPS)):
        back = lax.all_to_all(done[rotation], "inner", split_axis=0, concat_axis=0, tiled=True)
        if rotation > 0:
            back = shifted(back, "blk", rotation)
        back = back.reshape(group_count, SPLIT, half_cap, lanes_major, 128)
        combined = combined + jnp.einsum(
            "qcht,qchkl->tkl", scale_hi[rotation], back, preferred_element_type=jnp.float32
        )
        combined = combined + jnp.einsum(
            "qcht,qchkl->tkl", scale_lo[rotation], back, preferred_element_type=jnp.float32
        )
    combined = combined.reshape(tok_rows, width)
    return combined.astype(jnp.bfloat16)


def solution(mesh):
    return jax.shard_map(
        on_device,
        mesh=mesh,
        in_specs=(
            P(("blk", "inner"), None),
            P(("blk", "inner"), None),
            P(("blk", "inner"), None),
            P(("blk", "inner"), None, None),
            P(("blk", "inner"), None, None),
        ),
        out_specs=P(("blk", "inner"), None),
        check_vma=False,
    )
```

```python
import jax
import jax.numpy as jnp
from jax import lax
from jax.sharding import PartitionSpec as P

TOPK = 8
SPLIT = 2
STEPS = 3


def shifted(value, axis, steps):
    count = lax.axis_size(axis)
    pairs = [(source, (source + steps) % count) for source in range(count)]
    return lax.ppermute(value, axis, pairs)


def swapped_with_partner(value, axis):
    count = lax.axis_size(axis)
    pairs = [(source, source ^ 1) for source in range(count)]
    return lax.ppermute(value, axis, pairs)


def whole_expert(rows, w_in_a, w_out_a, w_in_b, w_out_b):
    hidden = w_out_a.shape[0]

    def one_half(w_in_now, w_out_now):
        projected = jnp.dot(rows, w_in_now, preferred_element_type=jnp.float32)
        activated = (jax.nn.silu(projected[:, :hidden]) * projected[:, hidden:]).astype(
            jnp.bfloat16
        )
        return jnp.dot(activated, w_out_now, preferred_element_type=jnp.float32)

    return (one_half(w_in_a, w_out_a) + one_half(w_in_b, w_out_b)).astype(jnp.bfloat16)


def on_device(tokens, expert_ids, route_weights, w_in, w_out):
    inner_count = lax.axis_size("inner")
    blk_count = lax.axis_size("blk")
    group_index = lax.axis_index("blk")
    group_count = inner_count // SPLIT
    tok_rows, width = tokens.shape
    experts_all = group_count * blk_count
    capacity = max(2, 3 * tok_rows * TOPK // (2 * experts_all))
    capacity = -(-capacity // SPLIT) * SPLIT
    half_cap = capacity // SPLIT

    w_in_other = swapped_with_partner(w_in, "inner")
    w_out_other = swapped_with_partner(w_out, "inner")

    homes = jnp.mod(group_index - jnp.arange(STEPS, dtype=jnp.int32), blk_count)
    targets = (
        homes[:, None] * group_count + jnp.arange(group_count, dtype=jnp.int32)[None, :]
    ).reshape(-1)
    matches = expert_ids[:, :, None] == targets[None, None, :]
    chosen = jnp.any(matches, axis=1).astype(jnp.int32)
    weighting = jnp.sum(jnp.where(matches, route_weights[:, :, None], 0.0), axis=1)
    position = jnp.cumsum(chosen, axis=0) - chosen
    slot_ids = jnp.arange(capacity, dtype=jnp.int32)
    one_hot = (chosen.T[:, None, :] == 1) & (position.T[:, None, :] == slot_ids[None, :, None])
    one_hot = one_hot.reshape(STEPS, group_count, SPLIT, half_cap, tok_rows)
    scale = jnp.where(
        one_hot, weighting.T.reshape(STEPS, group_count, 1, 1, tok_rows), 0.0
    )
    scale_hi = scale.astype(jnp.bfloat16)
    scale_lo = (scale - scale_hi.astype(jnp.float32)).astype(jnp.bfloat16)
    lanes_major = width // 128
    dense = tokens.reshape(tok_rows, lanes_major, 128)
    picked = jnp.einsum(
        "rqcht,tkl->rqchkl",
        one_hot.astype(jnp.bfloat16),
        dense,
        preferred_element_type=jnp.float32,
    ).astype(jnp.bfloat16)

    far = []
    for rotation in range(1, STEPS):
        outgoing = picked[rotation].reshape(inner_count, half_cap, lanes_major, 128)
        far.append(shifted(outgoing, "blk", -rotation))
    near = picked[0].reshape(inner_count, half_cap, lanes_major, 128)
    near = lax.all_to_all(near, "inner", split_axis=0, concat_axis=0, tiled=True)
    far = jnp.stack(far, axis=1)
    far = lax.all_to_all(far, "inner", split_axis=0, concat_axis=0, tiled=True)
    rows = jnp.concatenate(
        [near.reshape(-1, width), far.transpose(1, 0, 2, 3, 4).reshape(-1, width)], axis=0
    )
    done = whole_expert(rows, w_in[0], w_out[0], w_in_other[0], w_out_other[0])
    done = done.reshape(STEPS, inner_count, half_cap, lanes_major, 128)

    far_back = lax.all_to_all(
        done[1:].transpose(1, 0, 2, 3, 4), "inner", split_axis=0, concat_axis=0, tiled=True
    )
    near_back = lax.all_to_all(done[0], "inner", split_axis=0, concat_axis=0, tiled=True)
    backs = [near_back]
    for rotation in range(1, STEPS):
        backs.append(shifted(far_back[:, rotation - 1], "blk", rotation))

    combined = jnp.zeros((tok_rows, lanes_major, 128), jnp.float32)
    for rotation in range(STEPS):
        back = backs[rotation].reshape(group_count, SPLIT, half_cap, lanes_major, 128)
        combined = combined + jnp.einsum(
            "qcht,qchkl->tkl", scale_hi[rotation], back, preferred_element_type=jnp.float32
        )
        combined = combined + jnp.einsum(
            "qcht,qchkl->tkl", scale_lo[rotation], back, preferred_element_type=jnp.float32
        )
    combined = combined.reshape(tok_rows, width)
    return combined.astype(jnp.bfloat16)


def solution(mesh):
    return jax.shard_map(
        on_device,
        mesh=mesh,
        in_specs=(
            P(("blk", "inner"), None),
            P(("blk", "inner"), None),
            P(("blk", "inner"), None),
            P(("blk", "inner"), None, None),
            P(("blk", "inner"), None, None),
        ),
        out_specs=P(("blk", "inner"), None),
        check_vma=False,
    )
```

```python
import jax
import jax.numpy as jnp
from jax import lax
from jax.sharding import PartitionSpec as P

TOPK = 8
SPLIT = 2
STEPS = 3


def shifted(value, axis, steps):
    count = lax.axis_size(axis)
    pairs = [(source, (source + steps) % count) for source in range(count)]
    return lax.ppermute(value, axis, pairs)


def swapped_with_partner(value, axis):
    count = lax.axis_size(axis)
    pairs = [(source, source ^ 1) for source in range(count)]
    return lax.ppermute(value, axis, pairs)


def whole_expert(rows, w_in_a, w_out_a, w_in_b, w_out_b):
    hidden = w_out_a.shape[0]

    def one_half(w_in_now, w_out_now):
        projected = jnp.dot(rows, w_in_now, preferred_element_type=jnp.float32)
        activated = (jax.nn.silu(projected[:, :hidden]) * projected[:, hidden:]).astype(
            jnp.bfloat16
        )
        return jnp.dot(activated, w_out_now, preferred_element_type=jnp.float32)

    return (one_half(w_in_a, w_out_a) + one_half(w_in_b, w_out_b)).astype(jnp.bfloat16)


def on_device(tokens, expert_ids, route_weights, w_in, w_out):
    inner_count = lax.axis_size("inner")
    blk_count = lax.axis_size("blk")
    group_index = lax.axis_index("blk")
    group_count = inner_count // SPLIT
    tok_rows, width = tokens.shape
    experts_all = group_count * blk_count
    capacity = max(2, 3 * tok_rows * TOPK // (2 * experts_all))
    capacity = -(-capacity // SPLIT) * SPLIT
    half_cap = capacity // SPLIT

    w_in_other = swapped_with_partner(w_in, "inner")
    w_out_other = swapped_with_partner(w_out, "inner")

    homes = jnp.mod(group_index - jnp.arange(STEPS, dtype=jnp.int32), blk_count)
    targets = (
        homes[:, None] * group_count + jnp.arange(group_count, dtype=jnp.int32)[None, :]
    ).reshape(-1)
    matches = expert_ids[:, :, None] == targets[None, None, :]
    chosen = jnp.any(matches, axis=1).astype(jnp.int32)
    weighting = jnp.sum(jnp.where(matches, route_weights[:, :, None], 0.0), axis=1)
    position = jnp.cumsum(chosen, axis=0) - chosen
    slot_ids = jnp.arange(capacity, dtype=jnp.int32)
    one_hot = (chosen.T[:, None, :] == 1) & (position.T[:, None, :] == slot_ids[None, :, None])
    one_hot = one_hot.reshape(STEPS, group_count, SPLIT, half_cap, tok_rows)
    scale = jnp.where(
        one_hot, weighting.T.reshape(STEPS, group_count, 1, 1, tok_rows), 0.0
    )
    scale_hi = scale.astype(jnp.bfloat16)
    scale_lo = (scale - scale_hi.astype(jnp.float32)).astype(jnp.bfloat16)
    lanes_major = width // 128
    dense = tokens.reshape(tok_rows, lanes_major, 128)
    picked = jnp.einsum(
        "rqcht,tkl->rqchkl",
        one_hot.astype(jnp.bfloat16),
        dense,
        preferred_element_type=jnp.float32,
    ).astype(jnp.bfloat16)

    far = []
    for rotation in range(1, STEPS):
        outgoing = picked[rotation].reshape(inner_count, half_cap, lanes_major, 128)
        far.append(shifted(outgoing, "blk", -rotation))
    near = picked[0].reshape(inner_count, half_cap, lanes_major, 128)
    near = lax.all_to_all(near, "inner", split_axis=0, concat_axis=0, tiled=True)
    far = jnp.stack(far, axis=1)
    far = lax.all_to_all(far, "inner", split_axis=0, concat_axis=0, tiled=True)
    rows = jnp.concatenate(
        [near.reshape(-1, width), far.transpose(1, 0, 2, 3, 4).reshape(-1, width)], axis=0
    )
    done = whole_expert(rows, w_in[0], w_out[0], w_in_other[0], w_out_other[0])
    done = done.reshape(STEPS, inner_count, half_cap, lanes_major, 128)

    results = [done[0]]
    for rotation in range(1, STEPS):
        results.append(shifted(done[rotation], "blk", rotation))
    returned = jnp.stack(results, axis=1)
    returned = lax.all_to_all(returned, "inner", split_axis=0, concat_axis=0, tiled=True)
    returned = returned.reshape(group_count, SPLIT, STEPS, half_cap, lanes_major, 128)

    combined = jnp.einsum(
        "rqcht,qcrhkl->tkl", scale_hi, returned, preferred_element_type=jnp.float32
    ) + jnp.einsum("rqcht,qcrhkl->tkl", scale_lo, returned, preferred_element_type=jnp.float32)
    combined = combined.reshape(tok_rows, width)
    return combined.astype(jnp.bfloat16)


def solution(mesh):
    return jax.shard_map(
        on_device,
        mesh=mesh,
        in_specs=(
            P(("blk", "inner"), None),
            P(("blk", "inner"), None),
            P(("blk", "inner"), None),
            P(("blk", "inner"), None, None),
            P(("blk", "inner"), None, None),
        ),
        out_specs=P(("blk", "inner"), None),
        check_vma=False,
    )
```

```python
import jax
import jax.numpy as jnp
from jax import lax
from jax.sharding import PartitionSpec as P

TOPK = 8
SPLIT = 2
STEPS = 3


def shifted(value, axis, steps):
    count = lax.axis_size(axis)
    pairs = [(source, (source + steps) % count) for source in range(count)]
    return lax.ppermute(value, axis, pairs)


def one_step(value, axis, direction):
    count = lax.axis_size(axis)
    here = lax.axis_index(axis)

    def same_row(source):
        return source // 2 == ((source + direction) % count) // 2

    near = [s for s in range(count) if same_row(s)]
    far = [s for s in range(count) if not same_row(s)]
    direct = lax.ppermute(value, axis, [(s, (s + direction) % count) for s in near])
    half = value.shape[0] // 2
    first, second = value[:half], value[half:]
    first = lax.ppermute(first, axis, [(s, (s + 2 * direction) % count) for s in far])
    first = lax.ppermute(
        first, axis, [((s + 2 * direction) % count, (s + direction) % count) for s in far]
    )
    second = lax.ppermute(second, axis, [(s, (s - direction) % count) for s in far])
    second = lax.ppermute(
        second, axis, [((s - direction) % count, (s + direction) % count) for s in far]
    )
    routed = jnp.concatenate([first, second], axis=0)
    arrived_direct = ((here - direction) % count) // 2 == here // 2
    return jnp.where(arrived_direct, direct, routed)


def swapped_with_partner(value, axis):
    count = lax.axis_size(axis)
    pairs = [(source, source ^ 1) for source in range(count)]
    return lax.ppermute(value, axis, pairs)


def whole_expert(rows, w_in_a, w_out_a, w_in_b, w_out_b):
    hidden = w_out_a.shape[0]

    def one_half(w_in_now, w_out_now):
        projected = jnp.dot(rows, w_in_now, preferred_element_type=jnp.float32)
        activated = (jax.nn.silu(projected[:, :hidden]) * projected[:, hidden:]).astype(
            jnp.bfloat16
        )
        return jnp.dot(activated, w_out_now, preferred_element_type=jnp.float32)

    return (one_half(w_in_a, w_out_a) + one_half(w_in_b, w_out_b)).astype(jnp.bfloat16)


def on_device(tokens, expert_ids, route_weights, w_in, w_out):
    inner_count = lax.axis_size("inner")
    blk_count = lax.axis_size("blk")
    group_index = lax.axis_index("blk")
    group_count = inner_count // SPLIT
    tok_rows, width = tokens.shape
    experts_all = group_count * blk_count
    capacity = max(2, 3 * tok_rows * TOPK // (2 * experts_all))
    capacity = -(-capacity // SPLIT) * SPLIT
    half_cap = capacity // SPLIT

    w_in_other = swapped_with_partner(w_in, "inner")
    w_out_other = swapped_with_partner(w_out, "inner")

    homes = jnp.mod(group_index - jnp.arange(STEPS, dtype=jnp.int32), blk_count)
    targets = (
        homes[:, None] * group_count + jnp.arange(group_count, dtype=jnp.int32)[None, :]
    ).reshape(-1)
    matches = expert_ids[:, :, None] == targets[None, None, :]
    chosen = jnp.any(matches, axis=1).astype(jnp.int32)
    weighting = jnp.sum(jnp.where(matches, route_weights[:, :, None], 0.0), axis=1)
    position = jnp.cumsum(chosen, axis=0) - chosen
    slot_ids = jnp.arange(capacity, dtype=jnp.int32)
    one_hot = (chosen.T[:, None, :] == 1) & (position.T[:, None, :] == slot_ids[None, :, None])
    one_hot = one_hot.reshape(STEPS, group_count, SPLIT, half_cap, tok_rows)
    scale = jnp.where(
        one_hot, weighting.T.reshape(STEPS, group_count, 1, 1, tok_rows), 0.0
    )
    scale_hi = scale.astype(jnp.bfloat16)
    scale_lo = (scale - scale_hi.astype(jnp.float32)).astype(jnp.bfloat16)
    lanes_major = width // 128
    dense = tokens.reshape(tok_rows, lanes_major, 128)
    picked = jnp.einsum(
        "rqcht,tkl->rqchkl",
        one_hot.astype(jnp.bfloat16),
        dense,
        preferred_element_type=jnp.float32,
    ).astype(jnp.bfloat16)

    far = []
    for rotation in range(1, STEPS):
        outgoing = picked[rotation].reshape(inner_count, half_cap, lanes_major, 128)
        if rotation == 1:
            far.append(one_step(outgoing, "blk", -1))
        else:
            far.append(shifted(outgoing, "blk", -rotation))
    near = picked[0].reshape(inner_count, half_cap, lanes_major, 128)
    near = lax.all_to_all(near, "inner", split_axis=0, concat_axis=0, tiled=True)
    far = jnp.stack(far, axis=1)
    far = lax.all_to_all(far, "inner", split_axis=0, concat_axis=0, tiled=True)
    rows = jnp.concatenate(
        [near.reshape(-1, width), far.transpose(1, 0, 2, 3, 4).reshape(-1, width)], axis=0
    )
    done = whole_expert(rows, w_in[0], w_out[0], w_in_other[0], w_out_other[0])
    done = done.reshape(STEPS, inner_count, half_cap, lanes_major, 128)

    results = [done[0]]
    for rotation in range(1, STEPS):
        if rotation == 1:
            results.append(one_step(done[rotation], "blk", 1))
        else:
            results.append(shifted(done[rotation], "blk", rotation))
    returned = jnp.stack(results, axis=1)
    returned = lax.all_to_all(returned, "inner", split_axis=0, concat_axis=0, tiled=True)
    returned = returned.reshape(group_count, SPLIT, STEPS, half_cap, lanes_major, 128)

    combined = jnp.einsum(
        "rqcht,qcrhkl->tkl", scale_hi, returned, preferred_element_type=jnp.float32
    ) + jnp.einsum("rqcht,qcrhkl->tkl", scale_lo, returned, preferred_element_type=jnp.float32)
    combined = combined.reshape(tok_rows, width)
    return combined.astype(jnp.bfloat16)


def solution(mesh):
    return jax.shard_map(
        on_device,
        mesh=mesh,
        in_specs=(
            P(("blk", "inner"), None),
            P(("blk", "inner"), None),
            P(("blk", "inner"), None),
            P(("blk", "inner"), None, None),
            P(("blk", "inner"), None, None),
        ),
        out_specs=P(("blk", "inner"), None),
        check_vma=False,
    )
```

```python
import jax
import jax.numpy as jnp
from jax import lax
from jax.sharding import PartitionSpec as P

TOPK = 8
SPLIT = 2
STEPS = 3


def shifted(value, axis, steps):
    count = lax.axis_size(axis)
    pairs = [(source, (source + steps) % count) for source in range(count)]
    return lax.ppermute(value, axis, pairs)


def swapped_with_partner(value, axis):
    count = lax.axis_size(axis)
    pairs = [(source, source ^ 1) for source in range(count)]
    return lax.ppermute(value, axis, pairs)


def whole_expert(rows, w_in_a, w_out_a, w_in_b, w_out_b):
    hidden = w_out_a.shape[0]

    def one_half(w_in_now, w_out_now):
        projected = jnp.dot(rows, w_in_now, preferred_element_type=jnp.float32)
        activated = (jax.nn.silu(projected[:, :hidden]) * projected[:, hidden:]).astype(
            jnp.bfloat16
        )
        return jnp.dot(activated, w_out_now, preferred_element_type=jnp.float32)

    return (one_half(w_in_a, w_out_a) + one_half(w_in_b, w_out_b)).astype(jnp.bfloat16)


def on_device(tokens, expert_ids, route_weights, w_in, w_out):
    inner_count = lax.axis_size("inner")
    blk_count = lax.axis_size("blk")
    group_index = lax.axis_index("blk")
    group_count = inner_count // SPLIT
    tok_rows, width = tokens.shape
    experts_all = group_count * blk_count
    capacity = max(2, 3 * tok_rows * TOPK // (2 * experts_all))
    capacity = -(-capacity // SPLIT) * SPLIT
    half_cap = capacity // SPLIT

    w_in_other = swapped_with_partner(w_in, "inner")
    w_out_other = swapped_with_partner(w_out, "inner")

    homes = jnp.mod(group_index - jnp.arange(STEPS, dtype=jnp.int32), blk_count)
    targets = (
        homes[:, None] * group_count + jnp.arange(group_count, dtype=jnp.int32)[None, :]
    ).reshape(-1)
    matches = expert_ids[:, :, None] == targets[None, None, :]
    chosen = jnp.any(matches, axis=1).astype(jnp.int32)
    weighting = jnp.sum(jnp.where(matches, route_weights[:, :, None], 0.0), axis=1)
    position = jnp.cumsum(chosen, axis=0) - chosen
    slot_ids = jnp.arange(capacity, dtype=jnp.int32)
    one_hot = (chosen.T[:, None, :] == 1) & (position.T[:, None, :] == slot_ids[None, :, None])
    one_hot = one_hot.reshape(STEPS, group_count, SPLIT, half_cap, tok_rows)
    scale = jnp.where(
        one_hot, weighting.T.reshape(STEPS, group_count, 1, 1, tok_rows), 0.0
    )
    scale_hi = scale.astype(jnp.bfloat16)
    scale_lo = (scale - scale_hi.astype(jnp.float32)).astype(jnp.bfloat16)
    lanes_major = width // 128
    dense = tokens.reshape(tok_rows, lanes_major, 128)
    picked = jnp.einsum(
        "rqcht,tkl->rqchkl",
        one_hot.astype(jnp.bfloat16),
        dense,
        preferred_element_type=jnp.float32,
    ).astype(jnp.bfloat16)

    far = []
    for rotation in range(1, STEPS):
        outgoing = picked[rotation].reshape(inner_count, half_cap, lanes_major, 128)
        far.append(shifted(outgoing, "blk", -rotation))
    near = picked[0].reshape(inner_count, half_cap, lanes_major, 128)
    near = lax.all_to_all(near, "inner", split_axis=0, concat_axis=0, tiled=True)
    far = jnp.stack(far, axis=1)
    far = lax.all_to_all(far, "inner", split_axis=0, concat_axis=0, tiled=True)
    rows = jnp.concatenate(
        [near.reshape(-1, width), far.transpose(1, 0, 2, 3, 4).reshape(-1, width)], axis=0
    )
    done = whole_expert(rows, w_in[0], w_out[0], w_in_other[0], w_out_other[0])
    done = done.reshape(STEPS, inner_count, half_cap, lanes_major, 128)

    far_back = [shifted(done[rotation], "blk", rotation) for rotation in range(1, STEPS)]
    near_back = lax.all_to_all(done[0], "inner", split_axis=0, concat_axis=0, tiled=True)
    far_back = lax.all_to_all(
        jnp.stack(far_back, axis=1), "inner", split_axis=0, concat_axis=0, tiled=True
    )
    backs = [near_back] + [far_back[:, rotation - 1] for rotation in range(1, STEPS)]

    combined = jnp.zeros((tok_rows, lanes_major, 128), jnp.float32)
    for rotation in range(STEPS):
        back = backs[rotation].reshape(group_count, SPLIT, half_cap, lanes_major, 128)
        combined = combined + jnp.einsum(
            "qcht,qchkl->tkl", scale_hi[rotation], back, preferred_element_type=jnp.float32
        )
        combined = combined + jnp.einsum(
            "qcht,qchkl->tkl", scale_lo[rotation], back, preferred_element_type=jnp.float32
        )
    combined = combined.reshape(tok_rows, width)
    return combined.astype(jnp.bfloat16)


def solution(mesh):
    return jax.shard_map(
        on_device,
        mesh=mesh,
        in_specs=(
            P(("blk", "inner"), None),
            P(("blk", "inner"), None),
            P(("blk", "inner"), None),
            P(("blk", "inner"), None, None),
            P(("blk", "inner"), None, None),
        ),
        out_specs=P(("blk", "inner"), None),
        check_vma=False,
    )
```

```python
import jax
import jax.numpy as jnp
from jax import lax
from jax.sharding import PartitionSpec as P

TOPK = 8
SPLIT = 2
STEPS = 3


def shifted(value, axis, steps):
    count = lax.axis_size(axis)
    if steps % count == 0:
        return value
    pairs = [(source, (source + steps) % count) for source in range(count)]
    return lax.ppermute(value, axis, pairs)


def swapped_with_partner(value, axis):
    count = lax.axis_size(axis)
    pairs = [(source, source ^ 1) for source in range(count)]
    return lax.ppermute(value, axis, pairs)


def whole_expert(rows, w_in_a, w_out_a, w_in_b, w_out_b):
    hidden = w_out_a.shape[0]

    def one_half(w_in_now, w_out_now):
        projected = jnp.dot(rows, w_in_now, preferred_element_type=jnp.float32)
        activated = (jax.nn.silu(projected[:, :hidden]) * projected[:, hidden:]).astype(
            jnp.bfloat16
        )
        return jnp.dot(activated, w_out_now, preferred_element_type=jnp.float32)

    return (one_half(w_in_a, w_out_a) + one_half(w_in_b, w_out_b)).astype(jnp.bfloat16)


def on_device(tokens, expert_ids, route_weights, w_in, w_out):
    inner_count = lax.axis_size("inner")
    blk_count = lax.axis_size("blk")
    group_index = lax.axis_index("blk")
    group_count = inner_count // SPLIT
    tok_rows, width = tokens.shape
    experts_all = group_count * blk_count
    capacity = max(2, 3 * tok_rows * TOPK // (2 * experts_all))
    capacity = -(-capacity // SPLIT) * SPLIT
    half_cap = capacity // SPLIT

    w_in_other = swapped_with_partner(w_in, "inner")
    w_out_other = swapped_with_partner(w_out, "inner")

    homes = jnp.mod(group_index - jnp.arange(STEPS, dtype=jnp.int32), blk_count)
    targets = (
        homes[:, None] * group_count + jnp.arange(group_count, dtype=jnp.int32)[None, :]
    ).reshape(-1)
    matches = expert_ids[:, :, None] == targets[None, None, :]
    chosen = jnp.any(matches, axis=1).astype(jnp.int32)
    weighting = jnp.sum(jnp.where(matches, route_weights[:, :, None], 0.0), axis=1)
    position = jnp.cumsum(chosen, axis=0) - chosen
    slot_ids = jnp.arange(capacity, dtype=jnp.int32)
    one_hot = (chosen.T[:, None, :] == 1) & (position.T[:, None, :] == slot_ids[None, :, None])
    one_hot = one_hot.reshape(STEPS, group_count, SPLIT, half_cap, tok_rows)
    scale = jnp.where(
        one_hot, weighting.T.reshape(STEPS, group_count, 1, 1, tok_rows), 0.0
    )
    scale_hi = scale.astype(jnp.bfloat16)
    scale_lo = (scale - scale_hi.astype(jnp.float32)).astype(jnp.bfloat16)
    lanes_major = width // 128
    dense = tokens.reshape(tok_rows, lanes_major, 128)
    picked = jnp.einsum(
        "rqcht,tkl->rqchkl",
        one_hot.astype(jnp.bfloat16),
        dense,
        preferred_element_type=jnp.float32,
    ).astype(jnp.bfloat16)

    def exchanged(value):
        return lax.all_to_all(value, "inner", split_axis=0, concat_axis=0, tiled=True)

    outgoing = [
        picked[rotation].reshape(inner_count, half_cap, lanes_major, 128)
        for rotation in range(STEPS)
    ]
    arrived = [None] * STEPS
    for rotation in reversed(range(STEPS)):
        if rotation % 2 == 0:
            arrived[rotation] = exchanged(shifted(outgoing[rotation], "blk", -rotation))
        else:
            arrived[rotation] = shifted(exchanged(outgoing[rotation]), "blk", -rotation)
    rows = jnp.concatenate([part.reshape(-1, width) for part in arrived], axis=0)
    done = whole_expert(rows, w_in[0], w_out[0], w_in_other[0], w_out_other[0])
    done = done.reshape(STEPS, inner_count, half_cap, lanes_major, 128)

    backs = [None] * STEPS
    for rotation in reversed(range(STEPS)):
        if rotation % 2 == 0:
            backs[rotation] = exchanged(shifted(done[rotation], "blk", rotation))
        else:
            backs[rotation] = shifted(exchanged(done[rotation]), "blk", rotation)

    combined = jnp.zeros((tok_rows, lanes_major, 128), jnp.float32)
    for rotation in range(STEPS):
        back = backs[rotation].reshape(group_count, SPLIT, half_cap, lanes_major, 128)
        combined = combined + jnp.einsum(
            "qcht,qchkl->tkl", scale_hi[rotation], back, preferred_element_type=jnp.float32
        )
        combined = combined + jnp.einsum(
            "qcht,qchkl->tkl", scale_lo[rotation], back, preferred_element_type=jnp.float32
        )
    combined = combined.reshape(tok_rows, width)
    return combined.astype(jnp.bfloat16)


def solution(mesh):
    return jax.shard_map(
        on_device,
        mesh=mesh,
        in_specs=(
            P(("blk", "inner"), None),
            P(("blk", "inner"), None),
            P(("blk", "inner"), None),
            P(("blk", "inner"), None, None),
            P(("blk", "inner"), None, None),
        ),
        out_specs=P(("blk", "inner"), None),
        check_vma=False,
    )
```

```python
import jax
import jax.numpy as jnp
from jax import lax
from jax.sharding import PartitionSpec as P

TOPK = 8
SPLIT = 2
STEPS = 3


def shifted(value, axis, steps):
    count = lax.axis_size(axis)
    pairs = [(source, (source + steps) % count) for source in range(count)]
    return lax.ppermute(value, axis, pairs)


def swapped_with_partner(value, axis):
    count = lax.axis_size(axis)
    pairs = [(source, source ^ 1) for source in range(count)]
    return lax.ppermute(value, axis, pairs)


def whole_expert(rows, w_in_a, w_out_a, w_in_b, w_out_b):
    hidden = w_out_a.shape[0]

    def one_half(w_in_now, w_out_now):
        projected = jnp.dot(rows, w_in_now, preferred_element_type=jnp.float32)
        activated = (jax.nn.silu(projected[:, :hidden]) * projected[:, hidden:]).astype(
            jnp.bfloat16
        )
        return jnp.dot(activated, w_out_now, preferred_element_type=jnp.float32)

    return (one_half(w_in_a, w_out_a) + one_half(w_in_b, w_out_b)).astype(jnp.bfloat16)


def on_device(tokens, expert_ids, route_weights, w_in, w_out):
    inner_count = lax.axis_size("inner")
    blk_count = lax.axis_size("blk")
    group_index = lax.axis_index("blk")
    group_count = inner_count // SPLIT
    tok_rows, width = tokens.shape
    experts_all = group_count * blk_count
    capacity = max(2, 3 * tok_rows * TOPK // (2 * experts_all))
    capacity = -(-capacity // SPLIT) * SPLIT
    half_cap = capacity // SPLIT

    w_in_other = swapped_with_partner(w_in, "inner")
    w_out_other = swapped_with_partner(w_out, "inner")

    homes = jnp.mod(group_index - jnp.arange(STEPS, dtype=jnp.int32), blk_count)
    targets = (
        homes[:, None] * group_count + jnp.arange(group_count, dtype=jnp.int32)[None, :]
    ).reshape(-1)
    matches = expert_ids[:, :, None] == targets[None, None, :]
    chosen = jnp.any(matches, axis=1).astype(jnp.int32)
    weighting = jnp.sum(jnp.where(matches, route_weights[:, :, None], 0.0), axis=1)
    position = jnp.cumsum(chosen, axis=0) - chosen
    slot_ids = jnp.arange(capacity, dtype=jnp.int32)
    one_hot = (chosen.T[:, None, :] == 1) & (position.T[:, None, :] == slot_ids[None, :, None])
    one_hot = one_hot.reshape(STEPS, group_count, SPLIT, half_cap, tok_rows)
    scale = jnp.where(
        one_hot, weighting.T.reshape(STEPS, group_count, 1, 1, tok_rows), 0.0
    )
    scale_hi = scale.astype(jnp.bfloat16)
    scale_lo = (scale - scale_hi.astype(jnp.float32)).astype(jnp.bfloat16)
    lanes_major = width // 128
    dense = tokens.reshape(tok_rows, lanes_major, 128)
    picked = jnp.einsum(
        "rqcht,tkl->rqchkl",
        one_hot.astype(jnp.bfloat16),
        dense,
        preferred_element_type=jnp.float32,
    ).astype(jnp.bfloat16)

    def exchanged(value):
        return lax.all_to_all(value, "inner", split_axis=0, concat_axis=0, tiled=True)

    def far_in_halves(parts, direction):
        cut = half_cap // 2
        firsts = [part[:, :cut] for part in parts]
        seconds = [part[:, cut:] for part in parts]
        firsts = [
            shifted(first, "blk", direction * rotation)
            for rotation, first in enumerate(firsts, start=1)
        ]
        firsts, seconds = lax.optimization_barrier((firsts, seconds))
        seconds = [
            shifted(second, "blk", direction * rotation)
            for rotation, second in enumerate(seconds, start=1)
        ]
        firsts = jnp.split(exchanged(jnp.stack(firsts, axis=1)), len(parts), axis=1)
        seconds = jnp.split(exchanged(jnp.stack(seconds, axis=1)), len(parts), axis=1)
        firsts = [first[:, 0] for first in firsts]
        seconds = [second[:, 0] for second in seconds]
        return [
            jnp.concatenate([first, second], axis=1) for first, second in zip(firsts, seconds)
        ]

    outgoing = [
        picked[rotation].reshape(inner_count, half_cap, lanes_major, 128)
        for rotation in range(STEPS)
    ]
    near = exchanged(outgoing[0])
    arrived = [near] + far_in_halves(outgoing[1:], -1)
    rows = jnp.concatenate([part.reshape(-1, width) for part in arrived], axis=0)
    done = whole_expert(rows, w_in[0], w_out[0], w_in_other[0], w_out_other[0])
    done = done.reshape(STEPS, inner_count, half_cap, lanes_major, 128)

    near_back = exchanged(done[0])
    backs = [near_back] + far_in_halves([done[r] for r in range(1, STEPS)], 1)

    combined = jnp.zeros((tok_rows, lanes_major, 128), jnp.float32)
    for rotation in range(STEPS):
        back = backs[rotation].reshape(group_count, SPLIT, half_cap, lanes_major, 128)
        combined = combined + jnp.einsum(
            "qcht,qchkl->tkl", scale_hi[rotation], back, preferred_element_type=jnp.float32
        )
        combined = combined + jnp.einsum(
            "qcht,qchkl->tkl", scale_lo[rotation], back, preferred_element_type=jnp.float32
        )
    combined = combined.reshape(tok_rows, width)
    return combined.astype(jnp.bfloat16)


def solution(mesh):
    return jax.shard_map(
        on_device,
        mesh=mesh,
        in_specs=(
            P(("blk", "inner"), None),
            P(("blk", "inner"), None),
            P(("blk", "inner"), None),
            P(("blk", "inner"), None, None),
            P(("blk", "inner"), None, None),
        ),
        out_specs=P(("blk", "inner"), None),
        check_vma=False,
    )
```

```python
import jax
import jax.numpy as jnp
from jax import lax
from jax.sharding import PartitionSpec as P

TOPK = 8
SPLIT = 2
STEPS = 3


def shifted(value, axis, steps):
    count = lax.axis_size(axis)
    pairs = [(source, (source + steps) % count) for source in range(count)]
    return lax.ppermute(value, axis, pairs)


def swapped_with_partner(value, axis):
    count = lax.axis_size(axis)
    pairs = [(source, source ^ 1) for source in range(count)]
    return lax.ppermute(value, axis, pairs)


def whole_expert(rows, w_in_a, w_out_a, w_in_b, w_out_b):
    hidden = w_out_a.shape[0]

    def one_half(w_in_now, w_out_now):
        projected = jnp.dot(rows, w_in_now, preferred_element_type=jnp.float32)
        activated = (jax.nn.silu(projected[:, :hidden]) * projected[:, hidden:]).astype(
            jnp.bfloat16
        )
        return jnp.dot(activated, w_out_now, preferred_element_type=jnp.float32)

    return (one_half(w_in_a, w_out_a) + one_half(w_in_b, w_out_b)).astype(jnp.bfloat16)


def on_device(tokens, expert_ids, route_weights, w_in, w_out):
    inner_count = lax.axis_size("inner")
    blk_count = lax.axis_size("blk")
    group_index = lax.axis_index("blk")
    group_count = inner_count // SPLIT
    tok_rows, width = tokens.shape
    experts_all = group_count * blk_count
    capacity = max(2, 3 * tok_rows * TOPK // (2 * experts_all))
    capacity = -(-capacity // SPLIT) * SPLIT
    half_cap = capacity // SPLIT

    w_in_other = swapped_with_partner(w_in, "inner")
    w_out_other = swapped_with_partner(w_out, "inner")

    homes = jnp.mod(group_index - jnp.arange(STEPS, dtype=jnp.int32), blk_count)
    targets = (
        homes[:, None] * group_count + jnp.arange(group_count, dtype=jnp.int32)[None, :]
    ).reshape(-1)
    matches = expert_ids[:, :, None] == targets[None, None, :]
    chosen = jnp.any(matches, axis=1).astype(jnp.int32)
    weighting = jnp.sum(jnp.where(matches, route_weights[:, :, None], 0.0), axis=1)
    position = jnp.cumsum(chosen, axis=0) - chosen
    slot_ids = jnp.arange(capacity, dtype=jnp.int32)
    one_hot = (chosen.T[:, None, :] == 1) & (position.T[:, None, :] == slot_ids[None, :, None])
    one_hot = one_hot.reshape(STEPS, group_count, SPLIT, half_cap, tok_rows)
    scale = jnp.where(
        one_hot, weighting.T.reshape(STEPS, group_count, 1, 1, tok_rows), 0.0
    )
    scale_hi = scale.astype(jnp.bfloat16)
    scale_lo = (scale - scale_hi.astype(jnp.float32)).astype(jnp.bfloat16)
    lanes_major = width // 128
    dense = tokens.reshape(tok_rows, lanes_major, 128)
    picked = jnp.einsum(
        "rqcht,tkl->rqchkl",
        one_hot.astype(jnp.bfloat16),
        dense,
        preferred_element_type=jnp.float32,
    ).astype(jnp.bfloat16)

    far = []
    for rotation in range(1, STEPS):
        outgoing = picked[rotation].reshape(inner_count, half_cap, lanes_major, 128)
        far.append(shifted(outgoing, "blk", -rotation))
    near = picked[0].reshape(inner_count, half_cap, lanes_major, 128)
    near = lax.all_to_all(near, "inner", split_axis=0, concat_axis=0, tiled=True)
    far = jnp.stack(far, axis=1)
    far = lax.all_to_all(far, "inner", split_axis=0, concat_axis=0, tiled=True)
    near_done = whole_expert(
        near.reshape(-1, width), w_in[0], w_out[0], w_in_other[0], w_out_other[0]
    )
    far_done = whole_expert(
        far.transpose(1, 0, 2, 3, 4).reshape(-1, width),
        w_in[0],
        w_out[0],
        w_in_other[0],
        w_out_other[0],
    )
    done = jnp.concatenate([near_done, far_done], axis=0)
    done = done.reshape(STEPS, inner_count, half_cap, lanes_major, 128)

    far_back = [shifted(done[rotation], "blk", rotation) for rotation in range(1, STEPS)]
    near_back = lax.all_to_all(done[0], "inner", split_axis=0, concat_axis=0, tiled=True)
    far_back = lax.all_to_all(
        jnp.stack(far_back, axis=1), "inner", split_axis=0, concat_axis=0, tiled=True
    )
    backs = [near_back] + [far_back[:, rotation - 1] for rotation in range(1, STEPS)]

    combined = jnp.zeros((tok_rows, lanes_major, 128), jnp.float32)
    for rotation in range(STEPS):
        back = backs[rotation].reshape(group_count, SPLIT, half_cap, lanes_major, 128)
        combined = combined + jnp.einsum(
            "qcht,qchkl->tkl", scale_hi[rotation], back, preferred_element_type=jnp.float32
        )
        combined = combined + jnp.einsum(
            "qcht,qchkl->tkl", scale_lo[rotation], back, preferred_element_type=jnp.float32
        )
    combined = combined.reshape(tok_rows, width)
    return combined.astype(jnp.bfloat16)


def solution(mesh):
    return jax.shard_map(
        on_device,
        mesh=mesh,
        in_specs=(
            P(("blk", "inner"), None),
            P(("blk", "inner"), None),
            P(("blk", "inner"), None),
            P(("blk", "inner"), None, None),
            P(("blk", "inner"), None, None),
        ),
        out_specs=P(("blk", "inner"), None),
        check_vma=False,
    )
```

```python
import jax
import jax.numpy as jnp
from jax import lax
from jax.sharding import PartitionSpec as P

TOPK = 8
SPLIT = 2
STEPS = 3


def shifted(value, axis, steps):
    count = lax.axis_size(axis)
    pairs = [(source, (source + steps) % count) for source in range(count)]
    return lax.ppermute(value, axis, pairs)


def swapped_with_partner(value, axis):
    count = lax.axis_size(axis)
    pairs = [(source, source ^ 1) for source in range(count)]
    return lax.ppermute(value, axis, pairs)


def whole_expert(rows, w_in_a, w_out_a, w_in_b, w_out_b):
    hidden = w_out_a.shape[0]

    def one_half(w_in_now, w_out_now):
        projected = jnp.dot(rows, w_in_now, preferred_element_type=jnp.float32)
        activated = (jax.nn.silu(projected[:, :hidden]) * projected[:, hidden:]).astype(
            jnp.bfloat16
        )
        return jnp.dot(activated, w_out_now, preferred_element_type=jnp.float32)

    return (one_half(w_in_a, w_out_a) + one_half(w_in_b, w_out_b)).astype(jnp.bfloat16)


def on_device(tokens, expert_ids, route_weights, w_in, w_out):
    inner_count = lax.axis_size("inner")
    blk_count = lax.axis_size("blk")
    group_index = lax.axis_index("blk")
    group_count = inner_count // SPLIT
    tok_rows, width = tokens.shape
    experts_all = group_count * blk_count
    capacity = max(2, 3 * tok_rows * TOPK // (2 * experts_all))
    capacity = -(-capacity // SPLIT) * SPLIT
    half_cap = capacity // SPLIT

    w_in_other = swapped_with_partner(w_in, "inner")
    w_out_other = swapped_with_partner(w_out, "inner")

    homes = jnp.mod(group_index - jnp.arange(STEPS, dtype=jnp.int32), blk_count)
    targets = (
        homes[:, None] * group_count + jnp.arange(group_count, dtype=jnp.int32)[None, :]
    ).reshape(-1)
    matches = expert_ids[:, :, None] == targets[None, None, :]
    chosen = jnp.any(matches, axis=1).astype(jnp.int32)
    weighting = jnp.sum(jnp.where(matches, route_weights[:, :, None], 0.0), axis=1)
    position = jnp.cumsum(chosen, axis=0) - chosen
    slot_ids = jnp.arange(capacity, dtype=jnp.int32)
    one_hot = (chosen.T[:, None, :] == 1) & (position.T[:, None, :] == slot_ids[None, :, None])
    one_hot = one_hot.reshape(STEPS, group_count, SPLIT, half_cap, tok_rows)
    scale = jnp.where(
        one_hot, weighting.T.reshape(STEPS, group_count, 1, 1, tok_rows), 0.0
    )
    scale_hi = scale.astype(jnp.bfloat16)
    scale_lo = (scale - scale_hi.astype(jnp.float32)).astype(jnp.bfloat16)
    lanes_major = width // 128
    dense = tokens.reshape(tok_rows, lanes_major, 128)
    picked = jnp.einsum(
        "rqcht,tkl->rqchkl",
        one_hot.astype(jnp.bfloat16),
        dense,
        preferred_element_type=jnp.float32,
    ).astype(jnp.bfloat16)

    far = []
    for rotation in range(1, STEPS):
        outgoing = picked[rotation].reshape(inner_count, half_cap, lanes_major, 128)
        far.append(shifted(outgoing, "blk", -rotation))
    near = picked[0].reshape(inner_count, half_cap, lanes_major, 128)
    near = lax.all_to_all(near, "inner", split_axis=0, concat_axis=0, tiled=True)
    far = jnp.stack(far, axis=1)
    far = lax.all_to_all(far, "inner", split_axis=0, concat_axis=0, tiled=True)
    near_done = whole_expert(
        near.reshape(-1, width), w_in[0], w_out[0], w_in_other[0], w_out_other[0]
    )
    far_done = whole_expert(
        far.transpose(1, 0, 2, 3, 4).reshape(-1, width),
        w_in[0],
        w_out[0],
        w_in_other[0],
        w_out_other[0],
    )
    near_done, far_done = lax.optimization_barrier((near_done, far_done))
    done = jnp.concatenate([near_done, far_done], axis=0)
    done = done.reshape(STEPS, inner_count, half_cap, lanes_major, 128)

    far_back = [shifted(done[rotation], "blk", rotation) for rotation in range(1, STEPS)]
    near_back = lax.all_to_all(done[0], "inner", split_axis=0, concat_axis=0, tiled=True)
    far_back = lax.all_to_all(
        jnp.stack(far_back, axis=1), "inner", split_axis=0, concat_axis=0, tiled=True
    )
    backs = [near_back] + [far_back[:, rotation - 1] for rotation in range(1, STEPS)]

    combined = jnp.zeros((tok_rows, lanes_major, 128), jnp.float32)
    for rotation in range(STEPS):
        back = backs[rotation].reshape(group_count, SPLIT, half_cap, lanes_major, 128)
        combined = combined + jnp.einsum(
            "qcht,qchkl->tkl", scale_hi[rotation], back, preferred_element_type=jnp.float32
        )
        combined = combined + jnp.einsum(
            "qcht,qchkl->tkl", scale_lo[rotation], back, preferred_element_type=jnp.float32
        )
    combined = combined.reshape(tok_rows, width)
    return combined.astype(jnp.bfloat16)


def solution(mesh):
    return jax.shard_map(
        on_device,
        mesh=mesh,
        in_specs=(
            P(("blk", "inner"), None),
            P(("blk", "inner"), None),
            P(("blk", "inner"), None),
            P(("blk", "inner"), None, None),
            P(("blk", "inner"), None, None),
        ),
        out_specs=P(("blk", "inner"), None),
        check_vma=False,
    )
```

```python
import jax
import jax.numpy as jnp
from jax import lax
from jax.sharding import PartitionSpec as P

TOPK = 8
SPLIT = 2
STEPS = 3


def shifted(value, axis, steps):
    count = lax.axis_size(axis)
    pairs = [(source, (source + steps) % count) for source in range(count)]
    return lax.ppermute(value, axis, pairs)


def swapped_with_partner(value, axis):
    count = lax.axis_size(axis)
    pairs = [(source, source ^ 1) for source in range(count)]
    return lax.ppermute(value, axis, pairs)


def whole_expert(rows, w_in_a, w_out_a, w_in_b, w_out_b):
    hidden = w_out_a.shape[0]

    def one_half(w_in_now, w_out_now):
        projected = jnp.dot(rows, w_in_now, preferred_element_type=jnp.float32)
        activated = (jax.nn.silu(projected[:, :hidden]) * projected[:, hidden:]).astype(
            jnp.bfloat16
        )
        return jnp.dot(activated, w_out_now, preferred_element_type=jnp.float32)

    return (one_half(w_in_a, w_out_a) + one_half(w_in_b, w_out_b)).astype(jnp.bfloat16)


def on_device(tokens, expert_ids, route_weights, w_in, w_out):
    inner_count = lax.axis_size("inner")
    blk_count = lax.axis_size("blk")
    group_index = lax.axis_index("blk")
    group_count = inner_count // SPLIT
    tok_rows, width = tokens.shape
    experts_all = group_count * blk_count
    capacity = max(2, 3 * tok_rows * TOPK // (2 * experts_all))
    capacity = -(-capacity // SPLIT) * SPLIT
    half_cap = capacity // SPLIT

    w_in_other = swapped_with_partner(w_in, "inner")
    w_out_other = swapped_with_partner(w_out, "inner")

    homes = jnp.mod(group_index - jnp.arange(STEPS, dtype=jnp.int32), blk_count)
    targets = (
        homes[:, None] * group_count + jnp.arange(group_count, dtype=jnp.int32)[None, :]
    ).reshape(-1)
    matches = expert_ids[:, :, None] == targets[None, None, :]
    chosen = jnp.any(matches, axis=1).astype(jnp.int32)
    weighting = jnp.sum(jnp.where(matches, route_weights[:, :, None], 0.0), axis=1)
    position = jnp.cumsum(chosen, axis=0) - chosen
    slot_ids = jnp.arange(capacity, dtype=jnp.int32)
    one_hot = (chosen.T[:, None, :] == 1) & (position.T[:, None, :] == slot_ids[None, :, None])
    one_hot = one_hot.reshape(STEPS, group_count, SPLIT, half_cap, tok_rows)
    scale = jnp.where(
        one_hot, weighting.T.reshape(STEPS, group_count, 1, 1, tok_rows), 0.0
    )
    lanes_major = width // 128
    dense = tokens.reshape(tok_rows, lanes_major, 128)
    picked = jnp.einsum(
        "rqcht,tkl->rqchkl",
        one_hot.astype(jnp.bfloat16),
        dense,
        preferred_element_type=jnp.float32,
    ).astype(jnp.bfloat16)

    far = []
    for rotation in range(1, STEPS):
        outgoing = picked[rotation].reshape(inner_count, half_cap, lanes_major, 128)
        far.append(shifted(outgoing, "blk", -rotation))
    near = picked[0].reshape(inner_count, half_cap, lanes_major, 128)
    near = lax.all_to_all(near, "inner", split_axis=0, concat_axis=0, tiled=True)
    far = jnp.stack(far, axis=1)
    far = lax.all_to_all(far, "inner", split_axis=0, concat_axis=0, tiled=True)
    near_done = whole_expert(
        near.reshape(-1, width), w_in[0], w_out[0], w_in_other[0], w_out_other[0]
    )
    far_done = whole_expert(
        far.transpose(1, 0, 2, 3, 4).reshape(-1, width),
        w_in[0],
        w_out[0],
        w_in_other[0],
        w_out_other[0],
    )
    done = jnp.concatenate([near_done, far_done], axis=0)
    done = done.reshape(STEPS, inner_count, half_cap, lanes_major, 128)

    far_back = [shifted(done[rotation], "blk", rotation) for rotation in range(1, STEPS)]
    near_back = lax.all_to_all(done[0], "inner", split_axis=0, concat_axis=0, tiled=True)
    far_back = lax.all_to_all(
        jnp.stack(far_back, axis=1), "inner", split_axis=0, concat_axis=0, tiled=True
    )
    near_scale = scale[0].transpose(3, 0, 1, 2)
    far_scale = scale[1:].transpose(4, 1, 2, 0, 3)
    near_back = near_back.reshape(group_count, SPLIT, half_cap, lanes_major, 128)
    far_back = far_back.reshape(group_count, SPLIT, STEPS - 1, half_cap, lanes_major, 128)
    combined = jnp.zeros((tok_rows, lanes_major, 128), jnp.float32)
    for weights in (near_scale, near_scale - near_scale.astype(jnp.bfloat16).astype(jnp.float32)):
        combined = combined + jnp.einsum(
            "tqch,qchkl->tkl",
            weights.astype(jnp.bfloat16),
            near_back,
            preferred_element_type=jnp.float32,
        )
    for weights in (far_scale, far_scale - far_scale.astype(jnp.bfloat16).astype(jnp.float32)):
        combined = combined + jnp.einsum(
            "tqcrh,qcrhkl->tkl",
            weights.astype(jnp.bfloat16),
            far_back,
            preferred_element_type=jnp.float32,
        )
    combined = combined.reshape(tok_rows, width)
    return combined.astype(jnp.bfloat16)


def solution(mesh):
    return jax.shard_map(
        on_device,
        mesh=mesh,
        in_specs=(
            P(("blk", "inner"), None),
            P(("blk", "inner"), None),
            P(("blk", "inner"), None),
            P(("blk", "inner"), None, None),
            P(("blk", "inner"), None, None),
        ),
        out_specs=P(("blk", "inner"), None),
        check_vma=False,
    )
```

```python
import jax
import jax.numpy as jnp
from jax import lax
from jax.sharding import PartitionSpec as P

TOPK = 8
SPLIT = 2
STEPS = 3


def shifted(value, axis, steps):
    count = lax.axis_size(axis)
    pairs = [(source, (source + steps) % count) for source in range(count)]
    return lax.ppermute(value, axis, pairs)


def swapped_with_partner(value, axis):
    count = lax.axis_size(axis)
    pairs = [(source, source ^ 1) for source in range(count)]
    return lax.ppermute(value, axis, pairs)


def whole_expert(rows, w_in_a, w_out_a, w_in_b, w_out_b):
    hidden = w_out_a.shape[0]

    def one_half(w_in_now, w_out_now):
        projected = jnp.dot(rows, w_in_now, preferred_element_type=jnp.float32)
        activated = (jax.nn.silu(projected[:, :hidden]) * projected[:, hidden:]).astype(
            jnp.bfloat16
        )
        return jnp.dot(activated, w_out_now, preferred_element_type=jnp.float32)

    return (one_half(w_in_a, w_out_a) + one_half(w_in_b, w_out_b)).astype(jnp.bfloat16)


def on_device(tokens, expert_ids, route_weights, w_in, w_out):
    inner_count = lax.axis_size("inner")
    blk_count = lax.axis_size("blk")
    group_index = lax.axis_index("blk")
    group_count = inner_count // SPLIT
    tok_rows, width = tokens.shape
    experts_all = group_count * blk_count
    capacity = max(2, 3 * tok_rows * TOPK // (2 * experts_all))
    capacity = -(-capacity // SPLIT) * SPLIT
    half_cap = capacity // SPLIT

    w_in_other = swapped_with_partner(w_in, "inner")
    w_out_other = swapped_with_partner(w_out, "inner")

    homes = jnp.mod(group_index - jnp.arange(STEPS, dtype=jnp.int32), blk_count)
    targets = (
        homes[:, None] * group_count + jnp.arange(group_count, dtype=jnp.int32)[None, :]
    ).reshape(-1)
    matches = expert_ids[:, :, None] == targets[None, None, :]
    chosen = jnp.any(matches, axis=1).astype(jnp.int32)
    weighting = jnp.sum(jnp.where(matches, route_weights[:, :, None], 0.0), axis=1)
    position = jnp.cumsum(chosen, axis=0) - chosen
    slot_ids = jnp.arange(capacity, dtype=jnp.int32)
    one_hot = (chosen.T[:, None, :] == 1) & (position.T[:, None, :] == slot_ids[None, :, None])
    one_hot = one_hot.reshape(STEPS, group_count, SPLIT, half_cap, tok_rows)
    scale = jnp.where(
        one_hot, weighting.T.reshape(STEPS, group_count, 1, 1, tok_rows), 0.0
    )
    scale_hi = scale.astype(jnp.bfloat16)
    scale_lo = (scale - scale_hi.astype(jnp.float32)).astype(jnp.bfloat16)
    lanes_major = width // 128
    dense = tokens.reshape(tok_rows, lanes_major, 128)
    picked = jnp.einsum(
        "rqcht,tkl->rqchkl",
        one_hot.astype(jnp.bfloat16),
        dense,
        preferred_element_type=jnp.float32,
    ).astype(jnp.bfloat16)

    far = []
    for rotation in range(1, STEPS):
        outgoing = picked[rotation].reshape(inner_count, half_cap, lanes_major, 128)
        far.append(shifted(outgoing, "blk", -rotation))
    near = picked[0].reshape(inner_count, half_cap, lanes_major, 128)
    near = lax.all_to_all(near, "inner", split_axis=0, concat_axis=0, tiled=True)
    far = jnp.stack(far, axis=1)
    far = lax.all_to_all(far, "inner", split_axis=0, concat_axis=0, tiled=True)

    def expert_on(part):
        finished = whole_expert(
            part.reshape(-1, width), w_in[0], w_out[0], w_in_other[0], w_out_other[0]
        )
        return finished.reshape(inner_count, half_cap, lanes_major, 128)

    near_done = expert_on(near)
    far_back = [None] * (STEPS - 1)
    for rotation in reversed(range(1, STEPS)):
        far_back[rotation - 1] = shifted(expert_on(far[:, rotation - 1]), "blk", rotation)
    near_back = lax.all_to_all(near_done, "inner", split_axis=0, concat_axis=0, tiled=True)
    far_back = lax.all_to_all(
        jnp.stack(far_back, axis=1), "inner", split_axis=0, concat_axis=0, tiled=True
    )
    backs = [near_back] + [far_back[:, rotation - 1] for rotation in range(1, STEPS)]

    combined = jnp.zeros((tok_rows, lanes_major, 128), jnp.float32)
    for rotation in range(STEPS):
        back = backs[rotation].reshape(group_count, SPLIT, half_cap, lanes_major, 128)
        combined = combined + jnp.einsum(
            "qcht,qchkl->tkl", scale_hi[rotation], back, preferred_element_type=jnp.float32
        )
        combined = combined + jnp.einsum(
            "qcht,qchkl->tkl", scale_lo[rotation], back, preferred_element_type=jnp.float32
        )
    combined = combined.reshape(tok_rows, width)
    return combined.astype(jnp.bfloat16)


def solution(mesh):
    return jax.shard_map(
        on_device,
        mesh=mesh,
        in_specs=(
            P(("blk", "inner"), None),
            P(("blk", "inner"), None),
            P(("blk", "inner"), None),
            P(("blk", "inner"), None, None),
            P(("blk", "inner"), None, None),
        ),
        out_specs=P(("blk", "inner"), None),
        check_vma=False,
    )
```

```python
import jax
import jax.numpy as jnp
from jax import lax
from jax.sharding import PartitionSpec as P

TOPK = 8
SPLIT = 2
STEPS = 3


def shifted(value, axis, steps):
    count = lax.axis_size(axis)
    pairs = [(source, (source + steps) % count) for source in range(count)]
    return lax.ppermute(value, axis, pairs)


def swapped_with_partner(value, axis):
    count = lax.axis_size(axis)
    pairs = [(source, source ^ 1) for source in range(count)]
    return lax.ppermute(value, axis, pairs)


def whole_expert(rows, w_in_a, w_out_a, w_in_b, w_out_b):
    hidden = w_out_a.shape[0]

    def one_half(w_in_now, w_out_now):
        projected = jnp.dot(rows, w_in_now, preferred_element_type=jnp.float32)
        activated = (jax.nn.silu(projected[:, :hidden]) * projected[:, hidden:]).astype(
            jnp.bfloat16
        )
        return jnp.dot(activated, w_out_now, preferred_element_type=jnp.float32)

    return (one_half(w_in_a, w_out_a) + one_half(w_in_b, w_out_b)).astype(jnp.bfloat16)


def on_device(tokens, expert_ids, route_weights, w_in, w_out):
    inner_count = lax.axis_size("inner")
    blk_count = lax.axis_size("blk")
    group_index = lax.axis_index("blk")
    group_count = inner_count // SPLIT
    tok_rows, width = tokens.shape
    experts_all = group_count * blk_count
    capacity = max(2, 3 * tok_rows * TOPK // (2 * experts_all))
    capacity = -(-capacity // SPLIT) * SPLIT
    half_cap = capacity // SPLIT

    w_in_other = swapped_with_partner(w_in, "inner")
    w_out_other = swapped_with_partner(w_out, "inner")

    homes = jnp.mod(group_index - jnp.arange(STEPS, dtype=jnp.int32), blk_count)
    targets = (
        homes[:, None] * group_count + jnp.arange(group_count, dtype=jnp.int32)[None, :]
    ).reshape(-1)
    matches = expert_ids[:, :, None] == targets[None, None, :]
    chosen = jnp.any(matches, axis=1).astype(jnp.int32)
    weighting = jnp.sum(jnp.where(matches, route_weights[:, :, None], 0.0), axis=1)
    position = jnp.cumsum(chosen, axis=0) - chosen
    slot_ids = jnp.arange(capacity, dtype=jnp.int32)
    one_hot = (chosen.T[:, None, :] == 1) & (position.T[:, None, :] == slot_ids[None, :, None])
    one_hot = one_hot.reshape(STEPS, group_count, SPLIT, half_cap, tok_rows)
    scale = jnp.where(
        one_hot, weighting.T.reshape(STEPS, group_count, 1, 1, tok_rows), 0.0
    )
    scale_hi = scale.astype(jnp.bfloat16)
    scale_lo = (scale - scale_hi.astype(jnp.float32)).astype(jnp.bfloat16)
    lanes_major = width // 128
    dense = tokens.reshape(tok_rows, lanes_major, 128)
    picked = jnp.einsum(
        "rqcht,tkl->rqchkl",
        one_hot.astype(jnp.bfloat16),
        dense,
        preferred_element_type=jnp.float32,
    ).astype(jnp.bfloat16)

    far = []
    for rotation in range(1, STEPS):
        outgoing = picked[rotation].reshape(inner_count, half_cap, lanes_major, 128)
        far.append(shifted(outgoing, "blk", -rotation))
    near = picked[0].reshape(inner_count, half_cap, lanes_major, 128)
    near = lax.all_to_all(near, "inner", split_axis=0, concat_axis=0, tiled=True)
    far = jnp.stack(far, axis=1)
    far = lax.all_to_all(far, "inner", split_axis=0, concat_axis=0, tiled=True)
    near_done = whole_expert(
        near.reshape(-1, width), w_in[0], w_out[0], w_in_other[0], w_out_other[0]
    )
    far_done = whole_expert(
        far.transpose(1, 0, 2, 3, 4).reshape(-1, width),
        w_in[0],
        w_out[0],
        w_in_other[0],
        w_out_other[0],
    )
    done = jnp.concatenate([near_done, far_done], axis=0)
    done = done.reshape(STEPS, inner_count, half_cap, lanes_major, 128)

    results = [done[0]] + [shifted(done[r], "blk", r) for r in range(1, STEPS)]
    returned = lax.all_to_all(
        jnp.stack(results, axis=1), "inner", split_axis=0, concat_axis=0, tiled=True
    )
    returned = returned.reshape(group_count, SPLIT, STEPS, half_cap, lanes_major, 128)
    combined = jnp.einsum(
        "rqcht,qcrhkl->tkl", scale_hi, returned, preferred_element_type=jnp.float32
    ) + jnp.einsum("rqcht,qcrhkl->tkl", scale_lo, returned, preferred_element_type=jnp.float32)
    combined = combined.reshape(tok_rows, width)
    return combined.astype(jnp.bfloat16)


def solution(mesh):
    return jax.shard_map(
        on_device,
        mesh=mesh,
        in_specs=(
            P(("blk", "inner"), None),
            P(("blk", "inner"), None),
            P(("blk", "inner"), None),
            P(("blk", "inner"), None, None),
            P(("blk", "inner"), None, None),
        ),
        out_specs=P(("blk", "inner"), None),
        check_vma=False,
    )
```
